128 devices in a mesh: row: 64 (over y, z, x_lo, core), rep: 2 (over x_hi).
Axes of the slice: x: 4 (x_hi: 2, x_lo: 2; x = x_hi * 2 + x_lo), y: 4, z: 4, core: 2. Of those that a mesh axis runs over, the one named last changes fastest.
Arguments:
- out_grad: bfloat16 [65536, 256], P(('row', 'rep')), may hold values from -6 to 6
- relu_mask: int32 [65536, 256], P(('row', 'rep')), may hold values 0 or 1
- features: bfloat16 [65536, 256], P('row'), may hold values from -6 to 6
- weight: bfloat16 [256, 256], replicated, may hold values from -0.375 to 0.375
- tile_cols: int32 [512, 128], P('row', 'rep'), may hold values from 0 to 255, as said below
- tile_counts: int32 [512, 2], P('row', 'rep'), may hold values from 1 to 64
- tile_values: bfloat16 [512, 128, 128, 128], P('row', 'rep')
Outputs:
- grad_in: bfloat16 [65536, 256], P(('row', 'rep'))
- grad_weight: float32 [256, 256], replicated
The draws below stay inside these ranges and needn't reach their ends.
Inputs may be any that keep to these rules, and one draw needn't show every extreme that they name: `tile_cols`: the 64 entries of one row tile and one index of rep are distinct column tiles.
All inputs are finite; a program needn't handle non-finite values. No bound on the sum of `relu_mask` on one device may be relied on, other than what follows from the above.
Results may differ from the reference program's by a relative error of at most 0.0049.
Values may be sent and summed in bfloat16 or wider, within the bound.
No kernel may reach another device: no remote copies, remote signals or barrier semaphores. Data moves between devices by JAX's collectives and lax.ppermute only.
A program may use at most 320 MiB of HBM per device.

```python
import math
import jax
import jax.numpy as jnp
from jax import lax

FEAT = 256
TILE = 128
ROWS = 512
MAXT = 64
NODES = 65536
N_ROW = 64
N_REP = 2


def draw_tile_cols(key, part):
    total_lists = ROWS * N_ROW * N_REP // TILE * N_REP
    key_list = jax.random.split(key, total_lists)
    columns = jax.vmap(lambda single: jax.random.permutation(single, ROWS * N_ROW // TILE)[:MAXT])(key_list)
    return columns.reshape(ROWS * N_ROW * N_REP // TILE, N_REP * MAXT).astype(jnp.int32)


def draw_tile_counts(key, part):
    key_shift = jax.random.fold_in(key, 11)
    key_count = jax.random.fold_in(key, 12)
    key_full = jax.random.fold_in(key, 13)
    per_block = N_REP * ROWS // TILE
    halvings = jax.random.randint(key_shift, (N_ROW, 1, N_REP), 0, 4)
    ceiling = jnp.maximum(MAXT // jnp.power(2, halvings), 1)
    lowest = jnp.maximum(ceiling // 2, 1)
    counted = jax.random.randint(key_count, (N_ROW, per_block, N_REP), lowest, ceiling + 1)
    flattened = counted.reshape(-1)
    chosen = jax.random.randint(key_full, (), 0, flattened.shape[0])
    flattened = jnp.where(jnp.arange(flattened.shape[0]) == chosen, MAXT, flattened)
    return flattened.reshape(N_ROW * per_block, N_REP).astype(jnp.int32)


def draw_tile_values(key, part):
    key_base = jax.random.fold_in(key, 21)
    full_shape = (ROWS * N_ROW * N_REP // TILE, N_REP * MAXT, TILE, TILE)
    magnitude = 2.0 / math.sqrt(MAXT * TILE)
    uniform_part = jax.random.uniform(key_base, full_shape, jnp.float32, 0.05, 1.0)
    drawn = uniform_part * magnitude
    return drawn.astype(jnp.bfloat16)


def set_ends(values, own_key, low, largest):
    longest = values.shape.index(max(values.shape))
    spots = []
    for shift in (0, 1):
        where = [jax.random.randint(jax.random.fold_in(own_key, axis), (), 0, length) for axis, length in enumerate(values.shape)]
        where[longest] = (where[longest] + shift) % values.shape[longest]
        spots.append(tuple(where))
    return values.at[spots[0]].set(low).at[spots[1]].set(largest)


def steps_of(stream_key, dims, cuts, least, high):
    gain = 1.0
    for dim, blocks in cuts:
        draws = jax.random.uniform(jax.random.fold_in(jax.random.fold_in(stream_key, 6), dim), (blocks,), jnp.float32, least / len(cuts), high / len(cuts))
        gain = gain * jnp.repeat(jnp.exp(draws), dims[dim] // blocks).reshape((-1,) + (1,) * (len(dims) - 1 - dim))
    return gain


def gaussian(own_key, shape, width, bound, cuts=(), kind=jnp.bfloat16):
    entries = jax.random.normal(own_key, shape, jnp.float32) * width
    if len(cuts) > 0:
        entries = steps_of(own_key, shape, cuts, -0.22, 0.18) * entries
    return jnp.clip(entries, min=-bound, max=bound).astype(kind)


def setup_inputs(seed: int = 0) -> dict:
    keys = jax.random.split(jax.random.key(seed), 8)
    out_grad = gaussian(keys[0], (NODES, FEAT), 1.0, 6.0, ((0, 128),))
    relu_mask = set_ends((jax.random.randint(keys[1], (NODES, FEAT), 0, 2) < 1).astype(jnp.int32), jax.random.fold_in(keys[1], 1), 0, 1)
    features = gaussian(keys[2], (NODES, FEAT), 1.0, 6.0, ((0, 64),))
    weight = gaussian(keys[3], (FEAT, FEAT), FEAT ** -0.5, 0.375)
    tile_cols = draw_tile_cols(jax.random.fold_in(keys[7], 71), 0)
    tile_counts = draw_tile_counts(jax.random.fold_in(keys[7], 71), 0)
    tile_values = draw_tile_values(jax.random.fold_in(keys[7], 71), 0)
    return dict(out_grad=out_grad, relu_mask=relu_mask, features=features, weight=weight, tile_cols=tile_cols, tile_counts=tile_counts, tile_values=tile_values)


def reference(out_grad, relu_mask, features, weight, tile_cols, tile_counts, tile_values):
    gated = out_grad * relu_mask.astype(jnp.bfloat16)
    block_tiles = ROWS // TILE
    grad_tiles = gated.reshape(NODES // TILE, TILE, FEAT)
    slot_ids = jnp.arange(N_REP * MAXT, dtype=jnp.int32)
    replica = slot_ids // MAXT
    within = slot_ids % MAXT

    def one_row(inputs):
        values_row, column_ids, count_row = inputs
        active = within < count_row[replica]
        source = (column_ids // block_tiles * N_REP + replica) * block_tiles + column_ids % block_tiles
        picked = jnp.take(grad_tiles, source.astype(jnp.int32), axis=0).astype(jnp.float32)
        picked = jnp.where(active[:, None, None], picked, jnp.zeros((), jnp.float32))
        return jnp.einsum('sab,sbf->af', values_row.astype(jnp.float32), picked)
    propagated = lax.map(one_row, (tile_values, tile_cols, tile_counts)).reshape(NODES, FEAT)
    propagated_low = propagated.astype(jnp.bfloat16)
    grad_in = jnp.dot(propagated_low, weight.T, preferred_element_type=jnp.float32).astype(jnp.bfloat16)
    grad_weight = jnp.dot(features.astype(jnp.float32).T, propagated, precision=lax.Precision.HIGHEST) * (1.0 / math.sqrt(NODES))
    return (grad_in, grad_weight)
```

```python
import math

import jax
import jax.numpy as jnp
from jax import lax
from jax.sharding import PartitionSpec as P

AXES = ("row", "rep")
STAGES = ((1,), (2,), (3, 4), (5, 6), (0,))


def xor_pairs(count, mask):
    return [(i, i ^ mask) for i in range(count)]


def butterfly_sum(x):
    count = lax.axis_size("row") * lax.axis_size("rep")
    idx = lax.axis_index(AXES)
    buf = x
    for bits in STAGES:
        m = 1 << len(bits)
        pos = sum(((idx >> b) & 1) << i for i, b in enumerate(bits))
        parts = buf.reshape(m, buf.shape[0] // m, *buf.shape[1:])
        acc = jnp.take(parts, pos, axis=0)
        for d in range(1, m):
            mask = sum(((d >> i) & 1) << b for i, b in enumerate(bits))
            acc = acc + lax.ppermute(jnp.take(parts, pos ^ d, axis=0), AXES, xor_pairs(count, mask))
        buf = acc
    for bits in reversed(STAGES):
        m = 1 << len(bits)
        pos = sum(((idx >> b) & 1) << i for i, b in enumerate(bits))
        got = [buf]
        for d in range(1, m):
            mask = sum(((d >> i) & 1) << b for i, b in enumerate(bits))
            got.append(lax.ppermute(buf, AXES, xor_pairs(count, mask)))
        stacked = jnp.stack(got)
        order = jnp.arange(m, dtype=jnp.int32) ^ pos
        buf = jnp.take(stacked, order, axis=0).reshape(m * buf.shape[0], *buf.shape[1:])
    return buf


def shards(out_grad, relu_mask, features, weight, tile_cols, tile_counts, tile_values):
    own_rows, feature_width = out_grad.shape
    row_tiles, most_slots = tile_cols.shape
    tile_size = tile_values.shape[-1]
    block_tiles = own_rows // tile_size
    column_tiles = block_tiles * lax.axis_size("row")
    gated = out_grad * relu_mask.astype(jnp.bfloat16)
    active = jnp.arange(most_slots, dtype=jnp.int32)[None, :] < tile_counts
    gathered = lax.all_gather(gated, "row", axis=0, tiled=True)
    grad_tiles = gathered.reshape(column_tiles, tile_size, feature_width)
    picked = jnp.take(grad_tiles, tile_cols, axis=0)
    picked = jnp.where(active[:, :, None, None], picked, jnp.zeros((), jnp.bfloat16))
    partial_sum = jnp.einsum(
        "tsab,tsbf->taf", tile_values, picked, preferred_element_type=jnp.float32
    )
    partial_sum = partial_sum.reshape(row_tiles * tile_size, feature_width)
    node_count = own_rows * lax.axis_size("row") * lax.axis_size("rep")
    normalizer = 1.0 / math.sqrt(node_count)
    weight_term = jnp.dot(
        features.astype(jnp.float32).T, partial_sum, precision=lax.Precision.HIGHEST
    )
    grad_weight = butterfly_sum(weight_term * normalizer)
    rep = lax.axis_index("rep")
    halves = partial_sum.reshape(2, own_rows, feature_width)
    other = lax.ppermute(jnp.take(halves, 1 - rep, axis=0), "rep", [(0, 1), (1, 0)])
    propagated = jnp.take(halves, rep, axis=0) + other
    grad_in = jnp.dot(
        propagated.astype(jnp.bfloat16), weight.T, preferred_element_type=jnp.float32
    ).astype(jnp.bfloat16)
    return (grad_in, grad_weight)


def solution(mesh):
    in_specs = (
        P(("row", "rep"), None),
        P(("row", "rep"), None),
        P("row", None),
        P(),
        P("row", "rep"),
        P("row", "rep"),
        P("row", "rep", None, None),
    )
    out_specs = (P(("row", "rep"), None), P())
    return jax.shard_map(shards, mesh=mesh, in_specs=in_specs, out_specs=out_specs, check_vma=False)
```

```python
import math

import jax
import jax.numpy as jnp
from jax import lax
from jax.sharding import PartitionSpec as P

AXES = ("row", "rep")
CORE_BIT = 1
DOUBLING_STAGES = ((2, 0), (3, 4), (5, 6))


def xor_pairs(count, mask):
    return [(i, i ^ mask) for i in range(count)]


def group_mask(d, bits):
    return sum(((d >> i) & 1) << b for i, b in enumerate(bits))


def group_pos(idx, bits):
    return sum(((idx >> b) & 1) << i for i, b in enumerate(bits))


def butterfly_sum(x):
    count = lax.axis_size("row") * lax.axis_size("rep")
    idx = lax.axis_index(AXES)
    core = (idx >> CORE_BIT) & 1
    core_mask = 1 << CORE_BIT
    parts = x.reshape(2, x.shape[0] // 2, *x.shape[1:])
    mine = jnp.take(parts, core, axis=0)
    other = lax.ppermute(jnp.take(parts, 1 - core, axis=0), AXES, xor_pairs(count, core_mask))
    buf = jnp.where(core == 0, mine + other, other + mine)
    for bits in DOUBLING_STAGES:
        m = 1 << len(bits)
        pos = group_pos(idx, bits)
        got = [buf] + [
            lax.ppermute(buf, AXES, xor_pairs(count, group_mask(d, bits))) for d in range(1, m)
        ]
        ordered = jnp.take(jnp.stack(got), jnp.arange(m, dtype=jnp.int32) ^ pos, axis=0)
        buf = ordered[0]
        for j in range(1, m):
            buf = buf + ordered[j]
    got = lax.ppermute(buf, AXES, xor_pairs(count, core_mask))
    return jnp.where(core == 0, jnp.concatenate([buf, got]), jnp.concatenate([got, buf]))


def shards(out_grad, relu_mask, features, weight, tile_cols, tile_counts, tile_values):
    own_rows, feature_width = out_grad.shape
    row_tiles, most_slots = tile_cols.shape
    tile_size = tile_values.shape[-1]
    block_tiles = own_rows // tile_size
    column_tiles = block_tiles * lax.axis_size("row")
    gated = out_grad * relu_mask.astype(jnp.bfloat16)
    active = jnp.arange(most_slots, dtype=jnp.int32)[None, :] < tile_counts
    gathered = lax.all_gather(gated, "row", axis=0, tiled=True)
    grad_tiles = gathered.reshape(column_tiles, tile_size, feature_width)
    picked = jnp.take(grad_tiles, tile_cols, axis=0)
    picked = jnp.where(active[:, :, None, None], picked, jnp.zeros((), jnp.bfloat16))
    partial_sum = jnp.einsum(
        "tsab,tsbf->taf", tile_values, picked, preferred_element_type=jnp.float32
    )
    partial_sum = partial_sum.reshape(row_tiles * tile_size, feature_width)
    node_count = own_rows * lax.axis_size("row") * lax.axis_size("rep")
    normalizer = 1.0 / math.sqrt(node_count)
    weight_term = jnp.dot(
        features.astype(jnp.float32).T, partial_sum, precision=lax.Precision.HIGHEST
    )
    grad_weight = butterfly_sum(weight_term * normalizer)
    rep = lax.axis_index("rep")
    halves = partial_sum.reshape(2, own_rows, feature_width)
    other = lax.ppermute(jnp.take(halves, 1 - rep, axis=0), "rep", [(0, 1), (1, 0)])
    propagated = jnp.take(halves, rep, axis=0) + other
    grad_in = jnp.dot(
        propagated.astype(jnp.bfloat16), weight.T, preferred_element_type=jnp.float32
    ).astype(jnp.bfloat16)
    return (grad_in, grad_weight)


def solution(mesh):
    in_specs = (
        P(("row", "rep"), None),
        P(("row", "rep"), None),
        P("row", None),
        P(),
        P("row", "rep"),
        P("row", "rep"),
        P("row", "rep", None, None),
    )
    out_specs = (P(("row", "rep"), None), P())
    return jax.shard_map(shards, mesh=mesh, in_specs=in_specs, out_specs=out_specs, check_vma=False)
```

```python
import math

import jax
import jax.numpy as jnp
from jax import lax
from jax.experimental import pallas as pl
from jax.experimental.pallas import tpu as pltpu
from jax.sharding import PartitionSpec as P

AXES = ("row", "rep")
CORE_BIT = 1
DOUBLING_STAGES = ((2, 0), (3, 4), (5, 6))


def xor_pairs(count, mask):
    return [(i, i ^ mask) for i in range(count)]


def group_mask(d, bits):
    return sum(((d >> i) & 1) << b for i, b in enumerate(bits))


def group_pos(idx, bits):
    return sum(((idx >> b) & 1) << i for i, b in enumerate(bits))


def butterfly_sum(x):
    count = lax.axis_size("row") * lax.axis_size("rep")
    idx = lax.axis_index(AXES)
    core = (idx >> CORE_BIT) & 1
    core_mask = 1 << CORE_BIT
    parts = x.reshape(2, x.shape[0] // 2, *x.shape[1:])
    mine = jnp.take(parts, core, axis=0)
    other = lax.ppermute(jnp.take(parts, 1 - core, axis=0), AXES, xor_pairs(count, core_mask))
    buf = jnp.where(core == 0, mine + other, other + mine)
    for bits in DOUBLING_STAGES:
        m = 1 << len(bits)
        pos = group_pos(idx, bits)
        got = [buf] + [
            lax.ppermute(buf, AXES, xor_pairs(count, group_mask(d, bits))) for d in range(1, m)
        ]
        ordered = jnp.take(jnp.stack(got), jnp.arange(m, dtype=jnp.int32) ^ pos, axis=0)
        buf = ordered[0]
        for j in range(1, m):
            buf = buf + ordered[j]
    got = lax.ppermute(buf, AXES, xor_pairs(count, core_mask))
    return jnp.where(core == 0, jnp.concatenate([buf, got]), jnp.concatenate([got, buf]))


SLOT_GROUP = 16


def tile_kernel(cols_ref, counts_ref, values_ref, grad_ref, out_ref):
    t = pl.program_id(0)
    count = counts_ref[t, 0]
    slots = values_ref.shape[1]
    out_ref[...] = jnp.zeros(out_ref.shape, out_ref.dtype)
    for first in range(0, slots, SLOT_GROUP):

        @pl.when(count > first)
        def _():
            acc = jnp.zeros(out_ref.shape[1:], jnp.float32)
            for s in range(first, min(first + SLOT_GROUP, slots)):
                live = jnp.where(s < count, 1.0, 0.0).astype(jnp.float32)
                term = jnp.dot(
                    values_ref[0, s], grad_ref[cols_ref[t, s]], preferred_element_type=jnp.float32
                )
                acc = acc + term * live
            out_ref[0] += acc


def propagate_tiles(tile_cols, tile_counts, tile_values, grad_tiles):
    row_tiles, slots, tile_size, _ = tile_values.shape
    column_tiles, _, width = grad_tiles.shape
    grid_spec = pltpu.PrefetchScalarGridSpec(
        num_scalar_prefetch=2,
        grid=(row_tiles,),
        in_specs=[
            pl.BlockSpec((1, slots, tile_size, tile_size), lambda t, c, n: (t, 0, 0, 0)),
            pl.BlockSpec(
                (column_tiles, tile_size, width),
                lambda t, c, n: (0, 0, 0),
                pipeline_mode=pl.Buffered(1),
            ),
        ],
        out_specs=pl.BlockSpec((1, tile_size, width), lambda t, c, n: (t, 0, 0)),
    )
    flops = 2 * row_tiles * slots * tile_size * tile_size * width
    moved = tile_values.size * 2 + grad_tiles.size * 2 + row_tiles * tile_size * width * 4
    return pl.pallas_call(
        tile_kernel,
        out_shape=jax.ShapeDtypeStruct((row_tiles, tile_size, width), jnp.float32),
        grid_spec=grid_spec,
        compiler_params=pltpu.CompilerParams(
            dimension_semantics=("arbitrary",), vmem_limit_bytes=48 * 1024 * 1024
        ),
        cost_estimate=pl.CostEstimate(flops=flops, transcendentals=0, bytes_accessed=moved),
    )(tile_cols, tile_counts, tile_values, grad_tiles)


def shards(out_grad, relu_mask, features, weight, tile_cols, tile_counts, tile_values):
    own_rows, feature_width = out_grad.shape
    row_tiles, most_slots = tile_cols.shape
    tile_size = tile_values.shape[-1]
    block_tiles = own_rows // tile_size
    column_tiles = block_tiles * lax.axis_size("row")
    gated = out_grad * relu_mask.astype(jnp.bfloat16)
    gathered = lax.all_gather(gated, "row", axis=0, tiled=True)
    grad_tiles = gathered.reshape(column_tiles, tile_size, feature_width)
    partial_sum = propagate_tiles(tile_cols, tile_counts, tile_values, grad_tiles)
    partial_sum = partial_sum.reshape(row_tiles * tile_size, feature_width)
    node_count = own_rows * lax.axis_size("row") * lax.axis_size("rep")
    normalizer = 1.0 / math.sqrt(node_count)
    weight_term = jnp.dot(
        features.astype(jnp.float32).T, partial_sum, precision=lax.Precision.HIGHEST
    )
    grad_weight = butterfly_sum(weight_term * normalizer)
    rep = lax.axis_index("rep")
    halves = partial_sum.reshape(2, own_rows, feature_width)
    other = lax.ppermute(jnp.take(halves, 1 - rep, axis=0), "rep", [(0, 1), (1, 0)])
    propagated = jnp.take(halves, rep, axis=0) + other
    grad_in = jnp.dot(
        propagated.astype(jnp.bfloat16), weight.T, preferred_element_type=jnp.float32
    ).astype(jnp.bfloat16)
    return (grad_in, grad_weight)


def solution(mesh):
    in_specs = (
        P(("row", "rep"), None),
        P(("row", "rep"), None),
        P("row", None),
        P(),
        P("row", "rep"),
        P("row", "rep"),
        P("row", "rep", None, None),
    )
    out_specs = (P(("row", "rep"), None), P())
    return jax.shard_map(shards, mesh=mesh, in_specs=in_specs, out_specs=out_specs, check_vma=False)
```

```python
import math

import jax
import jax.numpy as jnp
from jax import lax
from jax.experimental import pallas as pl
from jax.experimental.pallas import tpu as pltpu
from jax.sharding import PartitionSpec as P

AXES = ("row", "rep")
CORE_BIT = 1
DOUBLING_STAGES = ((2, 0), (3, 4), (5, 6))


def xor_pairs(count, mask):
    return [(i, i ^ mask) for i in range(count)]


def group_mask(d, bits):
    return sum(((d >> i) & 1) << b for i, b in enumerate(bits))


def group_pos(idx, bits):
    return sum(((idx >> b) & 1) << i for i, b in enumerate(bits))


def butterfly_sum(x):
    count = lax.axis_size("row") * lax.axis_size("rep")
    idx = lax.axis_index(AXES)
    core = (idx >> CORE_BIT) & 1
    core_mask = 1 << CORE_BIT
    parts = x.reshape(2, x.shape[0] // 2, *x.shape[1:])
    mine = jnp.take(parts, core, axis=0)
    other = lax.ppermute(jnp.take(parts, 1 - core, axis=0), AXES, xor_pairs(count, core_mask))
    buf = jnp.where(core == 0, mine + other, other + mine)
    for bits in DOUBLING_STAGES:
        m = 1 << len(bits)
        pos = group_pos(idx, bits)
        got = [buf] + [
            lax.ppermute(buf, AXES, xor_pairs(count, group_mask(d, bits))) for d in range(1, m)
        ]
        ordered = jnp.take(jnp.stack(got), jnp.arange(m, dtype=jnp.int32) ^ pos, axis=0)
        buf = ordered[0]
        for j in range(1, m):
            buf = buf + ordered[j]
    got = lax.ppermute(buf, AXES, xor_pairs(count, core_mask))
    return jnp.where(core == 0, jnp.concatenate([buf, got]), jnp.concatenate([got, buf]))


SLOT_GROUP = 8


def tile_kernel(cols_ref, counts_ref, values_ref, grad_ref, out_ref):
    t = pl.program_id(0)
    count = counts_ref[t, 0]
    slots = values_ref.shape[1]
    out_ref[...] = jnp.zeros(out_ref.shape, out_ref.dtype)
    for first in range(0, slots, SLOT_GROUP):

        @pl.when(count > first)
        def _():
            acc = jnp.zeros(out_ref.shape[1:], jnp.float32)
            for s in range(first, min(first + SLOT_GROUP, slots)):
                live = jnp.where(s < count, 1.0, 0.0).astype(jnp.float32)
                term = jnp.dot(
                    values_ref[0, s], grad_ref[cols_ref[t, s]], preferred_element_type=jnp.float32
                )
                acc = acc + term * live
            out_ref[0] += acc


def propagate_tiles(tile_cols, tile_counts, tile_values, grad_tiles):
    row_tiles, slots, tile_size, _ = tile_values.shape
    column_tiles, _, width = grad_tiles.shape
    grid_spec = pltpu.PrefetchScalarGridSpec(
        num_scalar_prefetch=2,
        grid=(row_tiles,),
        in_specs=[
            pl.BlockSpec((1, slots, tile_size, tile_size), lambda t, c, n: (t, 0, 0, 0)),
            pl.BlockSpec(
                (column_tiles, tile_size, width),
                lambda t, c, n: (0, 0, 0),
                pipeline_mode=pl.Buffered(1),
            ),
        ],
        out_specs=pl.BlockSpec((1, tile_size, width), lambda t, c, n: (t, 0, 0)),
    )
    flops = 2 * row_tiles * slots * tile_size * tile_size * width
    moved = tile_values.size * 2 + grad_tiles.size * 2 + row_tiles * tile_size * width * 4
    return pl.pallas_call(
        tile_kernel,
        out_shape=jax.ShapeDtypeStruct((row_tiles, tile_size, width), jnp.float32),
        grid_spec=grid_spec,
        compiler_params=pltpu.CompilerParams(
            dimension_semantics=("arbitrary",), vmem_limit_bytes=48 * 1024 * 1024
        ),
        cost_estimate=pl.CostEstimate(flops=flops, transcendentals=0, bytes_accessed=moved),
    )(tile_cols, tile_counts, tile_values, grad_tiles)


def shards(out_grad, relu_mask, features, weight, tile_cols, tile_counts, tile_values):
    own_rows, feature_width = out_grad.shape
    row_tiles, most_slots = tile_cols.shape
    tile_size = tile_values.shape[-1]
    block_tiles = own_rows // tile_size
    column_tiles = block_tiles * lax.axis_size("row")
    gated = out_grad * relu_mask.astype(jnp.bfloat16)
    gathered = lax.all_gather(gated, "row", axis=0, tiled=True)
    grad_tiles = gathered.reshape(column_tiles, tile_size, feature_width)
    partial_sum = propagate_tiles(tile_cols, tile_counts, tile_values, grad_tiles)
    partial_sum = partial_sum.reshape(row_tiles * tile_size, feature_width)
    node_count = own_rows * lax.axis_size("row") * lax.axis_size("rep")
    normalizer = 1.0 / math.sqrt(node_count)
    weight_term = jnp.dot(
        features.astype(jnp.float32).T, partial_sum, precision=lax.Precision.HIGHEST
    )
    grad_weight = butterfly_sum(weight_term * normalizer)
    rep = lax.axis_index("rep")
    halves = partial_sum.reshape(2, own_rows, feature_width)
    other = lax.ppermute(jnp.take(halves, 1 - rep, axis=0), "rep", [(0, 1), (1, 0)])
    propagated = jnp.take(halves, rep, axis=0) + other
    grad_in = jnp.dot(
        propagated.astype(jnp.bfloat16), weight.T, preferred_element_type=jnp.float32
    ).astype(jnp.bfloat16)
    return (grad_in, grad_weight)


def solution(mesh):
    in_specs = (
        P(("row", "rep"), None),
        P(("row", "rep"), None),
        P("row", None),
        P(),
        P("row", "rep"),
        P("row", "rep"),
        P("row", "rep", None, None),
    )
    out_specs = (P(("row", "rep"), None), P())
    return jax.shard_map(shards, mesh=mesh, in_specs=in_specs, out_specs=out_specs, check_vma=False)
```

```python
import math

import jax
import jax.numpy as jnp
from jax import lax
from jax.experimental import pallas as pl
from jax.experimental.pallas import tpu as pltpu
from jax.sharding import PartitionSpec as P

AXES = ("row", "rep")
CORE_BIT = 1
DOUBLING_STAGES = ((2,), (3,), (4,), (5,), (6,), (0,))


def xor_pairs(count, mask):
    return [(i, i ^ mask) for i in range(count)]


def group_mask(d, bits):
    return sum(((d >> i) & 1) << b for i, b in enumerate(bits))


def group_pos(idx, bits):
    return sum(((idx >> b) & 1) << i for i, b in enumerate(bits))


def butterfly_sum(x):
    count = lax.axis_size("row") * lax.axis_size("rep")
    idx = lax.axis_index(AXES)
    core = (idx >> CORE_BIT) & 1
    core_mask = 1 << CORE_BIT
    parts = x.reshape(2, x.shape[0] // 2, *x.shape[1:])
    mine = jnp.take(parts, core, axis=0)
    other = lax.ppermute(jnp.take(parts, 1 - core, axis=0), AXES, xor_pairs(count, core_mask))
    buf = jnp.where(core == 0, mine + other, other + mine)
    for bits in DOUBLING_STAGES:
        m = 1 << len(bits)
        pos = group_pos(idx, bits)
        got = [buf] + [
            lax.ppermute(buf, AXES, xor_pairs(count, group_mask(d, bits))) for d in range(1, m)
        ]
        ordered = jnp.take(jnp.stack(got), jnp.arange(m, dtype=jnp.int32) ^ pos, axis=0)
        buf = ordered[0]
        for j in range(1, m):
            buf = buf + ordered[j]
    got = lax.ppermute(buf, AXES, xor_pairs(count, core_mask))
    return jnp.where(core == 0, jnp.concatenate([buf, got]), jnp.concatenate([got, buf]))


SLOT_GROUP = 16


def tile_kernel(cols_ref, counts_ref, values_ref, grad_ref, out_ref):
    t = pl.program_id(0)
    count = counts_ref[t, 0]
    slots = values_ref.shape[1]
    out_ref[...] = jnp.zeros(out_ref.shape, out_ref.dtype)
    for first in range(0, slots, SLOT_GROUP):

        @pl.when(count > first)
        def _():
            acc = jnp.zeros(out_ref.shape[1:], jnp.float32)
            for s in range(first, min(first + SLOT_GROUP, slots)):
                live = jnp.where(s < count, 1.0, 0.0).astype(jnp.float32)
                term = jnp.dot(
                    values_ref[0, s], grad_ref[cols_ref[t, s]], preferred_element_type=jnp.float32
                )
                acc = acc + term * live
            out_ref[0] += acc


def propagate_tiles(tile_cols, tile_counts, tile_values, grad_tiles):
    row_tiles, slots, tile_size, _ = tile_values.shape
    column_tiles, _, width = grad_tiles.shape
    grid_spec = pltpu.PrefetchScalarGridSpec(
        num_scalar_prefetch=2,
        grid=(row_tiles,),
        in_specs=[
            pl.BlockSpec((1, slots, tile_size, tile_size), lambda t, c, n: (t, 0, 0, 0)),
            pl.BlockSpec(
                (column_tiles, tile_size, width),
                lambda t, c, n: (0, 0, 0),
                pipeline_mode=pl.Buffered(1),
            ),
        ],
        out_specs=pl.BlockSpec((1, tile_size, width), lambda t, c, n: (t, 0, 0)),
    )
    flops = 2 * row_tiles * slots * tile_size * tile_size * width
    moved = tile_values.size * 2 + grad_tiles.size * 2 + row_tiles * tile_size * width * 4
    return pl.pallas_call(
        tile_kernel,
        out_shape=jax.ShapeDtypeStruct((row_tiles, tile_size, width), jnp.float32),
        grid_spec=grid_spec,
        compiler_params=pltpu.CompilerParams(
            dimension_semantics=("arbitrary",), vmem_limit_bytes=48 * 1024 * 1024
        ),
        cost_estimate=pl.CostEstimate(flops=flops, transcendentals=0, bytes_accessed=moved),
    )(tile_cols, tile_counts, tile_values, grad_tiles)


def shards(out_grad, relu_mask, features, weight, tile_cols, tile_counts, tile_values):
    own_rows, feature_width = out_grad.shape
    row_tiles, most_slots = tile_cols.shape
    tile_size = tile_values.shape[-1]
    block_tiles = own_rows // tile_size
    column_tiles = block_tiles * lax.axis_size("row")
    gated = out_grad * relu_mask.astype(jnp.bfloat16)
    gathered = lax.all_gather(gated, "row", axis=0, tiled=True)
    grad_tiles = gathered.reshape(column_tiles, tile_size, feature_width)
    partial_sum = propagate_tiles(tile_cols, tile_counts, tile_values, grad_tiles)
    partial_sum = partial_sum.reshape(row_tiles * tile_size, feature_width)
    node_count = own_rows * lax.axis_size("row") * lax.axis_size("rep")
    normalizer = 1.0 / math.sqrt(node_count)
    weight_term = jnp.dot(
        features.astype(jnp.float32).T, partial_sum, precision=lax.Precision.HIGHEST
    )
    grad_weight = butterfly_sum(weight_term * normalizer)
    rep = lax.axis_index("rep")
    halves = partial_sum.reshape(2, own_rows, feature_width)
    other = lax.ppermute(jnp.take(halves, 1 - rep, axis=0), "rep", [(0, 1), (1, 0)])
    propagated = jnp.take(halves, rep, axis=0) + other
    grad_in = jnp.dot(
        propagated.astype(jnp.bfloat16), weight.T, preferred_element_type=jnp.float32
    ).astype(jnp.bfloat16)
    return (grad_in, grad_weight)


def solution(mesh):
    in_specs = (
        P(("row", "rep"), None),
        P(("row", "rep"), None),
        P("row", None),
        P(),
        P("row", "rep"),
        P("row", "rep"),
        P("row", "rep", None, None),
    )
    out_specs = (P(("row", "rep"), None), P())
    return jax.shard_map(shards, mesh=mesh, in_specs=in_specs, out_specs=out_specs, check_vma=False)
```

```python
import math

import jax
import jax.numpy as jnp
from jax import lax
from jax.experimental import pallas as pl
from jax.experimental.pallas import tpu as pltpu
from jax.sharding import PartitionSpec as P

AXES = ("row", "rep")
CORE_BIT = 1
DOUBLING_STAGES = ((3, 4), (5, 6), (2, 0))


def xor_pairs(count, mask):
    return [(i, i ^ mask) for i in range(count)]


def group_mask(d, bits):
    return sum(((d >> i) & 1) << b for i, b in enumerate(bits))


def group_pos(idx, bits):
    return sum(((idx >> b) & 1) << i for i, b in enumerate(bits))


def butterfly_sum(x):
    count = lax.axis_size("row") * lax.axis_size("rep")
    idx = lax.axis_index(AXES)
    core = (idx >> CORE_BIT) & 1
    core_mask = 1 << CORE_BIT
    parts = x.reshape(2, x.shape[0] // 2, *x.shape[1:])
    mine = jnp.take(parts, core, axis=0)
    other = lax.ppermute(jnp.take(parts, 1 - core, axis=0), AXES, xor_pairs(count, core_mask))
    buf = jnp.where(core == 0, mine + other, other + mine)
    for bits in DOUBLING_STAGES:
        m = 1 << len(bits)
        pos = group_pos(idx, bits)
        got = [buf] + [
            lax.ppermute(buf, AXES, xor_pairs(count, group_mask(d, bits))) for d in range(1, m)
        ]
        ordered = jnp.take(jnp.stack(got), jnp.arange(m, dtype=jnp.int32) ^ pos, axis=0)
        buf = ordered[0]
        for j in range(1, m):
            buf = buf + ordered[j]
    got = lax.ppermute(buf, AXES, xor_pairs(count, core_mask))
    return jnp.where(core == 0, jnp.concatenate([buf, got]), jnp.concatenate([got, buf]))


SLOT_GROUP = 16


def tile_kernel(cols_ref, counts_ref, values_ref, grad_ref, out_ref):
    t = pl.program_id(0)
    count = counts_ref[t, 0]
    slots = values_ref.shape[1]
    out_ref[...] = jnp.zeros(out_ref.shape, out_ref.dtype)
    for first in range(0, slots, SLOT_GROUP):

        @pl.when(count > first)
        def _():
            acc = jnp.zeros(out_ref.shape[1:], jnp.float32)
            for s in range(first, min(first + SLOT_GROUP, slots)):
                live = jnp.where(s < count, 1.0, 0.0).astype(jnp.float32)
                term = jnp.dot(
                    values_ref[0, s], grad_ref[cols_ref[t, s]], preferred_element_type=jnp.float32
                )
                acc = acc + term * live
            out_ref[0] += acc


def propagate_tiles(tile_cols, tile_counts, tile_values, grad_tiles):
    row_tiles, slots, tile_size, _ = tile_values.shape
    column_tiles, _, width = grad_tiles.shape
    grid_spec = pltpu.PrefetchScalarGridSpec(
        num_scalar_prefetch=2,
        grid=(row_tiles,),
        in_specs=[
            pl.BlockSpec((1, slots, tile_size, tile_size), lambda t, c, n: (t, 0, 0, 0)),
            pl.BlockSpec(
                (column_tiles, tile_size, width),
                lambda t, c, n: (0, 0, 0),
                pipeline_mode=pl.Buffered(1),
            ),
        ],
        out_specs=pl.BlockSpec((1, tile_size, width), lambda t, c, n: (t, 0, 0)),
    )
    flops = 2 * row_tiles * slots * tile_size * tile_size * width
    moved = tile_values.size * 2 + grad_tiles.size * 2 + row_tiles * tile_size * width * 4
    return pl.pallas_call(
        tile_kernel,
        out_shape=jax.ShapeDtypeStruct((row_tiles, tile_size, width), jnp.float32),
        grid_spec=grid_spec,
        compiler_params=pltpu.CompilerParams(
            dimension_semantics=("arbitrary",), vmem_limit_bytes=48 * 1024 * 1024
        ),
        cost_estimate=pl.CostEstimate(flops=flops, transcendentals=0, bytes_accessed=moved),
    )(tile_cols, tile_counts, tile_values, grad_tiles)


def shards(out_grad, relu_mask, features, weight, tile_cols, tile_counts, tile_values):
    own_rows, feature_width = out_grad.shape
    row_tiles, most_slots = tile_cols.shape
    tile_size = tile_values.shape[-1]
    block_tiles = own_rows // tile_size
    column_tiles = block_tiles * lax.axis_size("row")
    gated = out_grad * relu_mask.astype(jnp.bfloat16)
    gathered = lax.all_gather(gated, "row", axis=0, tiled=True)
    grad_tiles = gathered.reshape(column_tiles, tile_size, feature_width)
    partial_sum = propagate_tiles(tile_cols, tile_counts, tile_values, grad_tiles)
    partial_sum = partial_sum.reshape(row_tiles * tile_size, feature_width)
    node_count = own_rows * lax.axis_size("row") * lax.axis_size("rep")
    normalizer = 1.0 / math.sqrt(node_count)
    weight_term = jnp.dot(
        features.astype(jnp.float32).T, partial_sum, precision=lax.Precision.HIGHEST
    )
    grad_weight = butterfly_sum(weight_term * normalizer)
    rep = lax.axis_index("rep")
    halves = partial_sum.reshape(2, own_rows, feature_width)
    other = lax.ppermute(jnp.take(halves, 1 - rep, axis=0), "rep", [(0, 1), (1, 0)])
    propagated = jnp.take(halves, rep, axis=0) + other
    grad_in = jnp.dot(
        propagated.astype(jnp.bfloat16), weight.T, preferred_element_type=jnp.float32
    ).astype(jnp.bfloat16)
    return (grad_in, grad_weight)


def solution(mesh):
    in_specs = (
        P(("row", "rep"), None),
        P(("row", "rep"), None),
        P("row", None),
        P(),
        P("row", "rep"),
        P("row", "rep"),
        P("row", "rep", None, None),
    )
    out_specs = (P(("row", "rep"), None), P())
    return jax.shard_map(shards, mesh=mesh, in_specs=in_specs, out_specs=out_specs, check_vma=False)
```

```python
import math

import jax
import jax.numpy as jnp
from jax import lax
from jax.experimental import pallas as pl
from jax.experimental.pallas import tpu as pltpu
from jax.sharding import PartitionSpec as P

AXES = ("row", "rep")
CORE_BIT = 1
DOUBLING_STAGES = ((2, 0), (3, 4), (5, 6))


def xor_pairs(count, mask):
    return [(i, i ^ mask) for i in range(count)]


def group_mask(d, bits):
    return sum(((d >> i) & 1) << b for i, b in enumerate(bits))


def group_pos(idx, bits):
    return sum(((idx >> b) & 1) << i for i, b in enumerate(bits))


def butterfly_sum(x):
    count = lax.axis_size("row") * lax.axis_size("rep")
    idx = lax.axis_index(AXES)
    core = (idx >> CORE_BIT) & 1
    core_mask = 1 << CORE_BIT
    parts = x.reshape(2, x.shape[0] // 2, *x.shape[1:])
    mine = jnp.take(parts, core, axis=0)
    other = lax.ppermute(jnp.take(parts, 1 - core, axis=0), AXES, xor_pairs(count, core_mask))
    buf = jnp.where(core == 0, mine + other, other + mine)
    for bits in DOUBLING_STAGES:
        m = 1 << len(bits)
        pos = group_pos(idx, bits)
        got = [buf] + [
            lax.ppermute(buf, AXES, xor_pairs(count, group_mask(d, bits))) for d in range(1, m)
        ]
        ordered = jnp.take(jnp.stack(got), jnp.arange(m, dtype=jnp.int32) ^ pos, axis=0)
        buf = ordered[0]
        for j in range(1, m):
            buf = buf + ordered[j]
    got = lax.ppermute(buf, AXES, xor_pairs(count, core_mask))
    return jnp.where(core == 0, jnp.concatenate([buf, got]), jnp.concatenate([got, buf]))


SLOT_GROUP = 32


def tile_kernel(cols_ref, counts_ref, values_ref, grad_ref, out_ref):
    t = pl.program_id(0)
    count = counts_ref[t, 0]
    slots = values_ref.shape[1]
    out_ref[...] = jnp.zeros(out_ref.shape, out_ref.dtype)
    for first in range(0, slots, SLOT_GROUP):

        @pl.when(count > first)
        def _():
            acc = jnp.zeros(out_ref.shape[1:], jnp.float32)
            for s in range(first, min(first + SLOT_GROUP, slots)):
                live = jnp.where(s < count, 1.0, 0.0).astype(jnp.float32)
                term = jnp.dot(
                    values_ref[0, s], grad_ref[cols_ref[t, s]], preferred_element_type=jnp.float32
                )
                acc = acc + term * live
            out_ref[0] += acc


def propagate_tiles(tile_cols, tile_counts, tile_values, grad_tiles):
    row_tiles, slots, tile_size, _ = tile_values.shape
    column_tiles, _, width = grad_tiles.shape
    grid_spec = pltpu.PrefetchScalarGridSpec(
        num_scalar_prefetch=2,
        grid=(row_tiles,),
        in_specs=[
            pl.BlockSpec((1, slots, tile_size, tile_size), lambda t, c, n: (t, 0, 0, 0)),
            pl.BlockSpec(
                (column_tiles, tile_size, width),
                lambda t, c, n: (0, 0, 0),
                pipeline_mode=pl.Buffered(1),
            ),
        ],
        out_specs=pl.BlockSpec((1, tile_size, width), lambda t, c, n: (t, 0, 0)),
    )
    flops = 2 * row_tiles * slots * tile_size * tile_size * width
    moved = tile_values.size * 2 + grad_tiles.size * 2 + row_tiles * tile_size * width * 4
    return pl.pallas_call(
        tile_kernel,
        out_shape=jax.ShapeDtypeStruct((row_tiles, tile_size, width), jnp.float32),
        grid_spec=grid_spec,
        compiler_params=pltpu.CompilerParams(
            dimension_semantics=("arbitrary",), vmem_limit_bytes=48 * 1024 * 1024
        ),
        cost_estimate=pl.CostEstimate(flops=flops, transcendentals=0, bytes_accessed=moved),
    )(tile_cols, tile_counts, tile_values, grad_tiles)


def shards(out_grad, relu_mask, features, weight, tile_cols, tile_counts, tile_values):
    own_rows, feature_width = out_grad.shape
    row_tiles, most_slots = tile_cols.shape
    tile_size = tile_values.shape[-1]
    block_tiles = own_rows // tile_size
    column_tiles = block_tiles * lax.axis_size("row")
    gated = out_grad * relu_mask.astype(jnp.bfloat16)
    gathered = lax.all_gather(gated, "row", axis=0, tiled=True)
    grad_tiles = gathered.reshape(column_tiles, tile_size, feature_width)
    partial_sum = propagate_tiles(tile_cols, tile_counts, tile_values, grad_tiles)
    partial_sum = partial_sum.reshape(row_tiles * tile_size, feature_width)
    node_count = own_rows * lax.axis_size("row") * lax.axis_size("rep")
    normalizer = 1.0 / math.sqrt(node_count)
    weight_term = jnp.dot(
        features.astype(jnp.float32).T, partial_sum, precision=lax.Precision.HIGHEST
    )
    grad_weight = butterfly_sum(weight_term * normalizer)
    rep = lax.axis_index("rep")
    halves = partial_sum.reshape(2, own_rows, feature_width)
    other = lax.ppermute(jnp.take(halves, 1 - rep, axis=0), "rep", [(0, 1), (1, 0)])
    propagated = jnp.take(halves, rep, axis=0) + other
    grad_in = jnp.dot(
        propagated.astype(jnp.bfloat16), weight.T, preferred_element_type=jnp.float32
    ).astype(jnp.bfloat16)
    return (grad_in, grad_weight)


def solution(mesh):
    in_specs = (
        P(("row", "rep"), None),
        P(("row", "rep"), None),
        P("row", None),
        P(),
        P("row", "rep"),
        P("row", "rep"),
        P("row", "rep", None, None),
    )
    out_specs = (P(("row", "rep"), None), P())
    return jax.shard_map(shards, mesh=mesh, in_specs=in_specs, out_specs=out_specs, check_vma=False)
```
